512 devices in a mesh: space: 64 (over x, y, core), rep: 8 (over z).
Axes of the slice: x: 4, y: 8, z: 8, core: 2. Of those that a mesh axis runs over, the one named last changes fastest.
Arguments:
- features: bfloat16 [8, 16384, 128], P('rep', 'space'), may hold values from -6 to 6
- cotangent: bfloat16 [8, 16384, 128], P('rep', 'space'), may hold values from -6 to 6
- point_owner: int32 [8, 16384], P('rep', 'space'), may hold values from 0 to 63, as said below
- point_slot: int32 [8, 16384], P('rep', 'space'), may hold values from 0 to 511, as said below
- block_links: int32 [8, 64, 26], P('rep', 'space'), may hold values from 0 to 1, as said below
- weights: bfloat16 [27, 128, 128], replicated, may hold values from -0.109375 to 0.109375
Outputs:
- out_features: bfloat16 [8, 16384, 128], P('rep', 'space')
- input_grad: bfloat16 [8, 16384, 128], P('rep', 'space')
- weight_grad: float32 [27, 128, 128], replicated
The draws below stay inside these ranges and needn't reach their ends.
Inputs may be any that keep to these rules, and one draw needn't show every extreme that they name: `point_owner`: among the points of one scan shard (256 consecutive rows of one replica), at most 8 have the same owner, and every scan shard has an owner that receives exactly 8 of its points. `point_slot`: within one replica, two points with the same owner never have the same slot. `block_links`: each slab is one block thick in x and has 3 x 3 block positions in y and z, each holding at most one of its blocks; slab o lies at x position o. Entry j names the block of slab o + dx at the neighbouring position, or 1 if no block is there or the slab is off the ends; the relation is symmetric (if b names c at offset d, c names b at offset -d).
All inputs are finite; a program needn't handle non-finite values.
Results may differ from the reference program's by a relative error of at most 0.001.
Values may be sent and summed in bfloat16 or wider, within the bound.
No kernel may reach another device: no remote copies, remote signals or barrier semaphores. Data moves between devices by JAX's collectives and lax.ppermute only.
A program may use at most 64 MiB of HBM per device.

```python
import math
import jax
import jax.numpy as jnp
from jax import lax

C = 128
GRID = 3
BLK_DEV = 1
PTS_DEV = 256
NPTS = 16384
ALLPTS = 131072
N_SPACE = 64
N_REP = 8


NEIGHBOR_OFFSETS = [(shift_x, shift_y, shift_z) for shift_x in (-1, 0, 1) for shift_y in (-1, 0, 1) for shift_z in (-1, 0, 1) if (shift_x, shift_y, shift_z) != (0, 0, 0)]


def route_tables(key):
    pool_size = BLK_DEV * 512
    capacity = pool_size // N_SPACE
    tokens = jnp.arange(pool_size, dtype=jnp.int32)

    def one_scan(subkey):
        key_hot, key_rank, key_order = jax.random.split(subkey, 3)
        hottest = jax.random.randint(key_hot, (), 0, N_SPACE)
        ranking = jax.random.permutation(key_rank, pool_size).astype(jnp.int32)
        ranking = jnp.where(tokens // capacity == hottest, ranking - pool_size, ranking)
        chosen = jnp.argsort(ranking, stable=True)[:PTS_DEV]
        return chosen[jax.random.permutation(key_order, PTS_DEV)].astype(jnp.int32)
    chosen_all = jax.vmap(one_scan)(jax.random.split(jax.random.fold_in(key, 11), N_REP * N_SPACE))
    chosen_all = chosen_all.reshape(N_REP, N_SPACE, PTS_DEV)
    owners = chosen_all // capacity
    within = chosen_all % capacity
    layouts = jax.vmap(lambda subkey: jax.random.permutation(subkey, pool_size))(jax.random.split(jax.random.fold_in(key, 12), N_REP * N_SPACE))
    layouts = layouts.astype(jnp.int32).reshape(N_REP, N_SPACE, pool_size)
    replica_ids = jnp.arange(N_REP)[:, None, None]
    sources = jnp.arange(N_SPACE)[None, :, None]
    slot_table = layouts[replica_ids, owners, sources * capacity + within]
    return (owners.reshape(N_REP, NPTS).astype(jnp.int32), slot_table.reshape(N_REP, NPTS).astype(jnp.int32))


def draw_point_owner(key, part):
    return route_tables(key)[0]


def draw_point_slot(key, part):
    return route_tables(key)[1]


def draw_block_links(key, part):
    spot_count = GRID * GRID
    subkeys = jax.random.split(jax.random.fold_in(key, 21), N_REP * N_SPACE)

    def one_slab(subkey):
        return jax.random.permutation(subkey, spot_count).astype(jnp.int32)[:BLK_DEV]
    places = jax.vmap(one_slab)(subkeys)
    places = places.astype(jnp.int32).reshape(N_REP, N_SPACE, BLK_DEV)
    place_y = places // GRID
    place_z = places % GRID
    devices = jnp.arange(N_SPACE, dtype=jnp.int32)
    columns = []
    for shift_x, shift_y, shift_z in NEIGHBOR_OFFSETS:
        target_y = place_y + shift_y
        target_z = place_z + shift_z
        inside = (target_y >= 0) & (target_y < GRID) & (target_z >= 0) & (target_z < GRID)
        wanted = target_y * GRID + target_z
        other_dev = jnp.clip(devices + shift_x, 0, N_SPACE - 1)
        dev_inside = (devices + shift_x >= 0) & (devices + shift_x < N_SPACE)
        others = places[:, other_dev, :]
        matched = (others[:, :, None, :] == wanted[:, :, :, None]) & inside[:, :, :, None] & dev_inside[None, :, None, None]
        present = jnp.any(matched, -1)
        first_hit = jnp.argmax(matched.astype(jnp.int32), -1).astype(jnp.int32)
        columns.append(jnp.where(present, first_hit, BLK_DEV).astype(jnp.int32))
    return jnp.stack(columns, -1).reshape(N_REP, N_SPACE * BLK_DEV, 26)


def steps_of(stream_key, dims, cuts, low, largest):
    loudness = 1.0
    for axis_at, blocks in cuts:
        steps = jax.random.uniform(jax.random.fold_in(jax.random.fold_in(stream_key, 6), axis_at), (blocks,), jnp.float32, low / len(cuts), largest / len(cuts))
        loudness = loudness * jnp.repeat(jnp.exp(steps), dims[axis_at] // blocks).reshape((-1,) + (1,) * (len(dims) - 1 - axis_at))
    return loudness


def bell_draw(key, shape, spread, reach, cuts=(), held_as=jnp.bfloat16):
    result = jax.random.normal(key, shape, jnp.float32) * spread
    if len(cuts) > 0:
        result = steps_of(key, shape, cuts, -0.22, 0.18) * result
    return jnp.clip(result, min=-reach, max=reach).astype(held_as)


def setup_inputs(seed: int = 0) -> dict:
    keys = jax.random.split(jax.random.key(seed), 7)
    return {
        "features": bell_draw(keys[0], (N_REP, NPTS, C), 1.0, 6.0, ((0, 8), (1, 64))),
        "cotangent": bell_draw(keys[1], (N_REP, NPTS, C), 1.0, 6.0, ((0, 8), (1, 64))),
        "point_owner": draw_point_owner(jax.random.fold_in(keys[6], 71), 0),
        "point_slot": draw_point_slot(jax.random.fold_in(keys[6], 71), 0),
        "block_links": draw_block_links(jax.random.fold_in(keys[6], 71), 0),
        "weights": bell_draw(keys[5], (27, C, C), (27 * C) ** -0.5, 0.109375),
    }


NEIGHBOR_OFFSETS = [(shift_x, shift_y, shift_z) for shift_x in (-1, 0, 1) for shift_y in (-1, 0, 1) for shift_z in (-1, 0, 1) if (shift_x, shift_y, shift_z) != (0, 0, 0)]
ALL_TAPS = [(shift_x, shift_y, shift_z) for shift_x in (-1, 0, 1) for shift_y in (-1, 0, 1) for shift_z in (-1, 0, 1)]

def extent(offset):
    if offset < 0:
        return (7, 8)
    if offset == 0:
        return (0, 8)
    return (0, 1)

def pad_blocks(blocks, low_faces, high_faces, slab_links):
    zero_block = jnp.zeros((1,) + blocks.shape[1:], blocks.dtype)
    zero_face = jnp.zeros((1,) + low_faces.shape[1:], low_faces.dtype)
    own_table = jnp.concatenate([blocks, zero_block], 0)
    low_table = jnp.concatenate([low_faces, zero_face], 0)
    high_table = jnp.concatenate([high_faces, zero_face], 0)
    slab_parts = []
    for shift_x in (-1, 0, 1):
        layers = []
        for shift_y in (-1, 0, 1):
            lower_y, upper_y = extent(shift_y)
            pieces = []
            for shift_z in (-1, 0, 1):
                lower_z, upper_z = extent(shift_z)
                if shift_x == 0 and shift_y == 0 and (shift_z == 0):
                    portion = blocks
                else:
                    column = slab_links[:, NEIGHBOR_OFFSETS.index((shift_x, shift_y, shift_z))]
                    if shift_x == 0:
                        portion = own_table[:, :, lower_y:upper_y, lower_z:upper_z][column]
                    elif shift_x < 0:
                        portion = low_table[:, lower_y:upper_y, lower_z:upper_z][column][:, None]
                    else:
                        portion = high_table[:, lower_y:upper_y, lower_z:upper_z][column][:, None]
                pieces.append(portion)
            layers.append(jnp.concatenate(pieces, 3))
        slab_parts.append(jnp.concatenate(layers, 2))
    return jnp.concatenate(slab_parts, 1)

def patch_columns(padded, direction):
    block_count = padded.shape[0]
    channels = padded.shape[-1]
    pieces = []
    for shift_x, shift_y, shift_z in ALL_TAPS:
        start_x = 1 + direction * shift_x
        start_y = 1 + direction * shift_y
        start_z = 1 + direction * shift_z
        pieces.append(padded[:, start_x:start_x + 8, start_y:start_y + 8, start_z:start_z + 8, :])
    return jnp.concatenate(pieces, -1).reshape(block_count * 512, 27 * channels)

def local_section(blocks_h, blocks_g, low_h, high_h, low_g, high_g, slab_links, weights):
    channels = weights.shape[-1]
    columns_h = patch_columns(pad_blocks(blocks_h, low_h, high_h, slab_links), 1)
    convolved = jnp.dot(columns_h, weights.reshape(27 * channels, channels), preferred_element_type=jnp.float32)
    columns_g = patch_columns(pad_blocks(blocks_g, low_g, high_g, slab_links), -1)
    flipped = jnp.transpose(weights, (0, 2, 1)).reshape(27 * channels, channels)
    backward = jnp.dot(columns_g, flipped, preferred_element_type=jnp.float32)
    grads_flat = blocks_g.reshape(-1, channels)
    grad_part = lax.dot_general(columns_h, grads_flat, (((0,), (0,)), ((), ())), preferred_element_type=jnp.float32)
    return (convolved, backward, grad_part)

def reference(features, cotangent, point_owner, point_slot, block_links, weights):
    channels = features.shape[-1]
    voxels = BLK_DEV * 512

    def replica(inputs):
        point_feats, point_grads, owners, point_slots, slab_links = inputs
        where_at = owners.astype(jnp.int32) * voxels + point_slots.astype(jnp.int32)
        dense_x = jnp.zeros((N_SPACE * voxels, channels), point_feats.dtype).at[where_at].set(point_feats)
        dense_g = jnp.zeros((N_SPACE * voxels, channels), point_grads.dtype).at[where_at].set(point_grads)
        dense_x = dense_x.reshape(N_SPACE, BLK_DEV, 8, 8, 8, channels)
        dense_g = dense_g.reshape(N_SPACE, BLK_DEV, 8, 8, 8, channels)
        hidden_all = jnp.maximum(dense_x, 0)
        links_all = slab_links.reshape(N_SPACE, BLK_DEV, 26)
        zero_faces = jnp.zeros((BLK_DEV, 8, 8, channels), point_feats.dtype)

        def owner_step(grad_sum, owner_index):
            blocks_x = dense_x[owner_index]
            blocks_g = dense_g[owner_index]
            blocks_h = hidden_all[owner_index]
            left_owner = jnp.maximum(owner_index - 1, 0)
            right_owner = jnp.minimum(owner_index + 1, N_SPACE - 1)
            low_h = jnp.where(owner_index > 0, hidden_all[left_owner][:, 7], zero_faces)
            high_h = jnp.where(owner_index < N_SPACE - 1, hidden_all[right_owner][:, 0], zero_faces)
            low_g = jnp.where(owner_index > 0, dense_g[left_owner][:, 7], zero_faces)
            high_g = jnp.where(owner_index < N_SPACE - 1, dense_g[right_owner][:, 0], zero_faces)
            convolved, backward, grad_part = local_section(blocks_h, blocks_g, low_h, high_h, low_g, high_g, links_all[owner_index], weights)
            flat_x = blocks_x.reshape(-1, channels)
            flat_g = blocks_g.reshape(-1, channels)
            out_x = (flat_x.astype(jnp.float32) + convolved).astype(point_feats.dtype)
            out_dx = (flat_g.astype(jnp.float32) + jnp.where(flat_x > 0, backward, 0.0)).astype(point_feats.dtype)
            return (grad_sum + grad_part, (out_x, out_dx))
        grad_sum, results = lax.scan(owner_step, jnp.zeros((27 * channels, channels), jnp.float32), jnp.arange(N_SPACE))
        result_x = results[0].reshape(N_SPACE * voxels, channels)[where_at]
        result_dx = results[1].reshape(N_SPACE * voxels, channels)[where_at]
        return (result_x, result_dx, grad_sum)
    results = lax.map(replica, (features, cotangent, point_owner, point_slot, block_links))
    weight_grad = (lax.optimization_barrier(jnp.sum(results[2], 0)) / math.sqrt(ALLPTS)).reshape(27, channels, channels)
    return (results[0], results[1], weight_grad)
```

```python
import math

import jax
import jax.numpy as jnp
import numpy as np
from jax import lax
from jax.sharding import Mesh
from jax.sharding import PartitionSpec as P

NEIGHBOR_OFFSETS = [
    (shift_x, shift_y, shift_z)
    for shift_x in (-1, 0, 1)
    for shift_y in (-1, 0, 1)
    for shift_z in (-1, 0, 1)
    if (shift_x, shift_y, shift_z) != (0, 0, 0)
]
ALL_TAPS = [
    (shift_x, shift_y, shift_z)
    for shift_x in (-1, 0, 1)
    for shift_y in (-1, 0, 1)
    for shift_z in (-1, 0, 1)
]
SPACE_AXES = ("sx", "sy", "sc")
REDUCE_ORDER = ("sc", "sx", "sy", "rep")


def extent(offset):
    if offset < 0:
        return (7, 8)
    if offset == 0:
        return (0, 8)
    return (0, 1)


def pad_blocks(blocks, low_faces, high_faces, slab_links):
    zero_block = jnp.zeros((1,) + blocks.shape[1:], blocks.dtype)
    zero_face = jnp.zeros((1,) + low_faces.shape[1:], low_faces.dtype)
    own_table = jnp.concatenate([blocks, zero_block], 0)
    low_table = jnp.concatenate([low_faces, zero_face], 0)
    high_table = jnp.concatenate([high_faces, zero_face], 0)
    slab_parts = []
    for shift_x in (-1, 0, 1):
        layers = []
        for shift_y in (-1, 0, 1):
            lower_y, upper_y = extent(shift_y)
            pieces = []
            for shift_z in (-1, 0, 1):
                lower_z, upper_z = extent(shift_z)
                if shift_x == 0 and shift_y == 0 and (shift_z == 0):
                    portion = blocks
                else:
                    column = slab_links[:, NEIGHBOR_OFFSETS.index((shift_x, shift_y, shift_z))]
                    if shift_x == 0:
                        portion = own_table[:, :, lower_y:upper_y, lower_z:upper_z][column]
                    elif shift_x < 0:
                        portion = low_table[:, lower_y:upper_y, lower_z:upper_z][column][:, None]
                    else:
                        portion = high_table[:, lower_y:upper_y, lower_z:upper_z][column][:, None]
                pieces.append(portion)
            layers.append(jnp.concatenate(pieces, 3))
        slab_parts.append(jnp.concatenate(layers, 2))
    return jnp.concatenate(slab_parts, 1)


def patch_columns(padded, direction):
    block_count = padded.shape[0]
    channels = padded.shape[-1]
    pieces = []
    for shift_x, shift_y, shift_z in ALL_TAPS:
        start_x = 1 + direction * shift_x
        start_y = 1 + direction * shift_y
        start_z = 1 + direction * shift_z
        pieces.append(
            padded[:, start_x : start_x + 8, start_y : start_y + 8, start_z : start_z + 8, :]
        )
    return jnp.concatenate(pieces, -1).reshape(block_count * 512, 27 * channels)


def reduce_everywhere(value, sizes):
    flat = value.reshape(-1)
    for axis in REDUCE_ORDER:
        count = sizes[axis]
        lanes = 128 if flat.shape[0] % (count * 128) == 0 else flat.shape[0] // count
        parts = lax.all_to_all(flat.reshape(count, -1, lanes), axis, 0, 0, tiled=True)
        flat = jnp.sum(parts, 0).reshape(-1)
    for axis in reversed(REDUCE_ORDER):
        count = sizes[axis]
        lanes = 128 if flat.shape[0] % 128 == 0 else flat.shape[0]
        spread = jnp.broadcast_to(flat.reshape(1, -1, lanes), (count, flat.shape[0] // lanes, lanes))
        flat = lax.all_to_all(spread, axis, 0, 0, tiled=True).reshape(-1)
    return flat.reshape(value.shape)


def make_local(sizes):
    def local(features, cotangent, point_owner, point_slot, block_links, weights):
        peer_count = sizes["sx"] * sizes["sy"] * sizes["sc"]
        rep_count = sizes["rep"]
        channels = features.shape[-1]
        data_type = features.dtype
        links_here = block_links[0]
        blocks_here = links_here.shape[0]
        voxels = blocks_here * 512
        capacity = voxels // peer_count
        owners = point_owner[0]
        slots_here = point_slot[0]
        matches = (owners[:, None] == jnp.arange(peer_count, dtype=jnp.int32)[None, :]).astype(
            jnp.int32
        )
        earlier = jnp.cumsum(matches, axis=0) - matches
        within = jnp.sum(earlier * matches, axis=1)
        bucket = owners * capacity + within
        payload = jnp.concatenate([features[0], cotangent[0]], -1)
        rows = (
            jnp.zeros((peer_count * capacity, 2 * channels), data_type)
            .at[bucket]
            .set(payload)
            .reshape(peer_count, capacity * 2 * channels)
        )
        slot_full = (
            jnp.full((peer_count * capacity,), voxels, jnp.int32)
            .at[bucket]
            .set(slots_here)
            .reshape(peer_count, capacity)
        )
        slot_hi = (slot_full // 32).astype(data_type)
        slot_lo = (slot_full % 32).astype(data_type)
        slot_row = jnp.concatenate(
            [
                slot_hi,
                slot_lo,
                jnp.zeros((peer_count, 2 * channels - 2 * capacity), data_type),
            ],
            -1,
        )
        send = jnp.concatenate([rows, slot_row], -1)
        recv = lax.all_to_all(send, SPACE_AXES, 0, 0, tiled=True)
        recv_rows = recv[:, : capacity * 2 * channels].reshape(peer_count * capacity, 2 * channels)
        recv_slot = recv[:, capacity * 2 * channels :]
        arrived = (
            recv_slot[:, :capacity].astype(jnp.int32) * 32
            + recv_slot[:, capacity : 2 * capacity].astype(jnp.int32)
        ).reshape(-1)
        dense = (
            jnp.zeros((voxels + 1, 2 * channels), data_type).at[arrived].set(recv_rows)[:voxels]
        )
        dense_x = dense[:, :channels]
        dense_g = dense[:, channels:]
        block_shape = (blocks_here, 8, 8, 8, channels)
        blocks_x = dense_x.reshape(block_shape)
        blocks_h = jnp.maximum(blocks_x, 0)
        blocks_g = dense_g.reshape(block_shape)
        faces = jnp.concatenate(
            [blocks_h[:, 0], blocks_g[:, 0], blocks_h[:, 7], blocks_g[:, 7]], -1
        )
        up = [(i, (i + 1) % peer_count) for i in range(peer_count - 1)]
        down = [(j, i) for i, j in up]
        from_below = lax.ppermute(faces[..., 2 * channels :], SPACE_AXES, up)
        from_above = lax.ppermute(faces[..., : 2 * channels], SPACE_AXES, down)
        low_h, low_g = from_below[..., :channels], from_below[..., channels:]
        high_h, high_g = from_above[..., :channels], from_above[..., channels:]
        columns_h = patch_columns(pad_blocks(blocks_h, low_h, high_h, links_here), 1)
        columns_g = patch_columns(pad_blocks(blocks_g, low_g, high_g, links_here), -1)
        grads_flat = dense_g
        grad_part = lax.dot_general(
            columns_h, grads_flat, (((0,), (0,)), ((), ())), preferred_element_type=jnp.float32
        )
        convolved = jnp.dot(
            columns_h,
            weights.reshape(27 * channels, channels),
            preferred_element_type=jnp.float32,
        )
        flipped = jnp.transpose(weights, (0, 2, 1)).reshape(27 * channels, channels)
        backward = jnp.dot(columns_g, flipped, preferred_element_type=jnp.float32)
        out_x = (dense_x.astype(jnp.float32) + convolved).astype(data_type)
        out_dx = (dense_g.astype(jnp.float32) + jnp.where(dense_x > 0, backward, 0.0)).astype(
            data_type
        )
        out_both = jnp.concatenate(
            [jnp.concatenate([out_x, out_dx], -1), jnp.zeros((1, 2 * channels), data_type)], 0
        )
        ret = out_both[arrived].reshape(peer_count, capacity * 2 * channels)
        home = lax.all_to_all(ret, SPACE_AXES, 0, 0, tiled=True).reshape(-1, 2 * channels)
        final = home[bucket]
        final_x = final[:, :channels]
        final_dx = final[:, channels:]
        summed = reduce_everywhere(grad_part, sizes)
        norm_scale = 1.0 / math.sqrt(peer_count * rep_count * owners.shape[0])
        weight_grad = (summed * norm_scale).reshape(27, channels, channels)
        return (final_x[None], final_dx[None], weight_grad)

    return local


def split_space(mesh):
    grid = np.asarray(mesh.devices)
    space_count = grid.shape[0]
    try:
        column = grid[:, 0]
        xs = len({int(d.coords[0]) for d in column})
        cores = len({int(d.core_on_chip) for d in column})
    except Exception:
        cores = 2
        xs = 4
    ys = space_count // (xs * cores)
    return xs, ys, cores


def solution(mesh):
    xs, ys, cores = split_space(mesh)
    grid = np.asarray(mesh.devices)
    rep_count = grid.shape[1]
    fine = Mesh(grid.reshape(xs, ys, cores, rep_count), ("sx", "sy", "sc", "rep"))
    sizes = {"sx": xs, "sy": ys, "sc": cores, "rep": rep_count}
    space = SPACE_AXES
    in_specs = (
        P("rep", space, None),
        P("rep", space, None),
        P("rep", space),
        P("rep", space),
        P("rep", space, None),
        P(),
    )
    out_specs = (P("rep", space, None), P("rep", space, None), P())
    return jax.shard_map(
        make_local(sizes), mesh=fine, in_specs=in_specs, out_specs=out_specs, check_vma=False
    )
```

```python
import math

import jax
import jax.numpy as jnp
import numpy as np
from jax import lax
from jax.sharding import Mesh
from jax.sharding import PartitionSpec as P

NEIGHBOR_OFFSETS = [
    (shift_x, shift_y, shift_z)
    for shift_x in (-1, 0, 1)
    for shift_y in (-1, 0, 1)
    for shift_z in (-1, 0, 1)
    if (shift_x, shift_y, shift_z) != (0, 0, 0)
]
ALL_TAPS = [
    (shift_x, shift_y, shift_z)
    for shift_x in (-1, 0, 1)
    for shift_y in (-1, 0, 1)
    for shift_z in (-1, 0, 1)
]
SPACE_AXES = ("sx", "sy", "sc")
REDUCE_ORDER = ("sc", "sx", "sy", "rep")


def extent(offset):
    if offset < 0:
        return (7, 8)
    if offset == 0:
        return (0, 8)
    return (0, 1)


def pad_blocks(blocks, low_faces, high_faces, slab_links):
    zero_block = jnp.zeros((1,) + blocks.shape[1:], blocks.dtype)
    zero_face = jnp.zeros((1,) + low_faces.shape[1:], low_faces.dtype)
    own_table = jnp.concatenate([blocks, zero_block], 0)
    low_table = jnp.concatenate([low_faces, zero_face], 0)
    high_table = jnp.concatenate([high_faces, zero_face], 0)
    slab_parts = []
    for shift_x in (-1, 0, 1):
        layers = []
        for shift_y in (-1, 0, 1):
            lower_y, upper_y = extent(shift_y)
            pieces = []
            for shift_z in (-1, 0, 1):
                lower_z, upper_z = extent(shift_z)
                if shift_x == 0 and shift_y == 0 and (shift_z == 0):
                    portion = blocks
                else:
                    column = slab_links[:, NEIGHBOR_OFFSETS.index((shift_x, shift_y, shift_z))]
                    if shift_x == 0:
                        portion = own_table[:, :, lower_y:upper_y, lower_z:upper_z][column]
                    elif shift_x < 0:
                        portion = low_table[:, lower_y:upper_y, lower_z:upper_z][column][:, None]
                    else:
                        portion = high_table[:, lower_y:upper_y, lower_z:upper_z][column][:, None]
                pieces.append(portion)
            layers.append(jnp.concatenate(pieces, 3))
        slab_parts.append(jnp.concatenate(layers, 2))
    return jnp.concatenate(slab_parts, 1)


def patch_columns(padded, direction):
    block_count = padded.shape[0]
    channels = padded.shape[-1]
    pieces = []
    for shift_x, shift_y, shift_z in ALL_TAPS:
        start_x = 1 + direction * shift_x
        start_y = 1 + direction * shift_y
        start_z = 1 + direction * shift_z
        pieces.append(
            padded[:, start_x : start_x + 8, start_y : start_y + 8, start_z : start_z + 8, :]
        )
    return jnp.concatenate(pieces, -1).reshape(block_count * 512, 27 * channels)


def tap_view(padded, shift_x, shift_y, shift_z, direction):
    channels = padded.shape[-1]
    start_x = 1 + direction * shift_x
    start_y = 1 + direction * shift_y
    start_z = 1 + direction * shift_z
    return padded[
        :, start_x : start_x + 8, start_y : start_y + 8, start_z : start_z + 8, :
    ].reshape(-1, channels)


def reduce_everywhere(value, sizes):
    flat = value.reshape(-1)
    for axis in REDUCE_ORDER:
        count = sizes[axis]
        lanes = 128 if flat.shape[0] % (count * 128) == 0 else flat.shape[0] // count
        parts = lax.all_to_all(flat.reshape(count, -1, lanes), axis, 0, 0, tiled=True)
        flat = jnp.sum(parts, 0).reshape(-1)
    for axis in reversed(REDUCE_ORDER):
        count = sizes[axis]
        lanes = 128 if flat.shape[0] % 128 == 0 else flat.shape[0]
        spread = jnp.broadcast_to(flat.reshape(1, -1, lanes), (count, flat.shape[0] // lanes, lanes))
        flat = lax.all_to_all(spread, axis, 0, 0, tiled=True).reshape(-1)
    return flat.reshape(value.shape)


def make_local(sizes):
    def local(features, cotangent, point_owner, point_slot, block_links, weights):
        peer_count = sizes["sx"] * sizes["sy"] * sizes["sc"]
        rep_count = sizes["rep"]
        channels = features.shape[-1]
        data_type = features.dtype
        links_here = block_links[0]
        blocks_here = links_here.shape[0]
        voxels = blocks_here * 512
        capacity = voxels // peer_count
        owners = point_owner[0]
        slots_here = point_slot[0]
        matches = (owners[:, None] == jnp.arange(peer_count, dtype=jnp.int32)[None, :]).astype(
            jnp.int32
        )
        earlier = jnp.cumsum(matches, axis=0) - matches
        within = jnp.sum(earlier * matches, axis=1)
        bucket = owners * capacity + within
        payload = jnp.concatenate([features[0], cotangent[0]], -1)
        rows = (
            jnp.zeros((peer_count * capacity, 2 * channels), data_type)
            .at[bucket]
            .set(payload)
            .reshape(peer_count, capacity * 2 * channels)
        )
        slot_full = (
            jnp.full((peer_count * capacity,), voxels, jnp.int32)
            .at[bucket]
            .set(slots_here)
            .reshape(peer_count, capacity)
        )
        slot_hi = (slot_full // 32).astype(data_type)
        slot_lo = (slot_full % 32).astype(data_type)
        slot_row = jnp.concatenate(
            [
                slot_hi,
                slot_lo,
                jnp.zeros((peer_count, 2 * channels - 2 * capacity), data_type),
            ],
            -1,
        )
        send = jnp.concatenate([rows, slot_row], -1)
        recv = lax.all_to_all(send, SPACE_AXES, 0, 0, tiled=True)
        recv_rows = recv[:, : capacity * 2 * channels].reshape(peer_count * capacity, 2 * channels)
        recv_slot = recv[:, capacity * 2 * channels :]
        arrived = (
            recv_slot[:, :capacity].astype(jnp.int32) * 32
            + recv_slot[:, capacity : 2 * capacity].astype(jnp.int32)
        ).reshape(-1)
        dense = (
            jnp.zeros((voxels + 1, 2 * channels), data_type).at[arrived].set(recv_rows)[:voxels]
        )
        dense_x = dense[:, :channels]
        dense_g = dense[:, channels:]
        block_shape = (blocks_here, 8, 8, 8, channels)
        blocks_x = dense_x.reshape(block_shape)
        blocks_h = jnp.maximum(blocks_x, 0)
        blocks_g = dense_g.reshape(block_shape)
        faces = jnp.concatenate(
            [blocks_h[:, 0], blocks_g[:, 0], blocks_h[:, 7], blocks_g[:, 7]], -1
        )
        up = [(i, (i + 1) % peer_count) for i in range(peer_count - 1)]
        down = [(j, i) for i, j in up]
        from_below = lax.ppermute(faces[..., 2 * channels :], SPACE_AXES, up)
        from_above = lax.ppermute(faces[..., : 2 * channels], SPACE_AXES, down)
        low_h, low_g = from_below[..., :channels], from_below[..., channels:]
        high_h, high_g = from_above[..., :channels], from_above[..., channels:]
        padded_h = pad_blocks(blocks_h, low_h, high_h, links_here)
        padded_g = pad_blocks(blocks_g, low_g, high_g, links_here)
        grads_flat = dense_g
        tap_grads = []
        for shift_x, shift_y, shift_z in ALL_TAPS:
            view_h = tap_view(padded_h, shift_x, shift_y, shift_z, 1)
            tap_grads.append(
                lax.dot_general(
                    view_h, grads_flat, (((0,), (0,)), ((), ())), preferred_element_type=jnp.float32
                )
            )
        grad_part = jnp.stack(tap_grads, 0)
        convolved = jnp.zeros((voxels, channels), jnp.float32)
        backward = jnp.zeros((voxels, channels), jnp.float32)
        for tap_index, (shift_x, shift_y, shift_z) in enumerate(ALL_TAPS):
            view_h = tap_view(padded_h, shift_x, shift_y, shift_z, 1)
            view_g = tap_view(padded_g, shift_x, shift_y, shift_z, -1)
            tap_weight = weights[tap_index]
            convolved = convolved + jnp.dot(view_h, tap_weight, preferred_element_type=jnp.float32)
            backward = backward + lax.dot_general(
                view_g, tap_weight, (((1,), (1,)), ((), ())), preferred_element_type=jnp.float32
            )
        out_x = (dense_x.astype(jnp.float32) + convolved).astype(data_type)
        out_dx = (dense_g.astype(jnp.float32) + jnp.where(dense_x > 0, backward, 0.0)).astype(
            data_type
        )
        out_both = jnp.concatenate(
            [jnp.concatenate([out_x, out_dx], -1), jnp.zeros((1, 2 * channels), data_type)], 0
        )
        ret = out_both[arrived].reshape(peer_count, capacity * 2 * channels)
        home = lax.all_to_all(ret, SPACE_AXES, 0, 0, tiled=True).reshape(-1, 2 * channels)
        final = home[bucket]
        final_x = final[:, :channels]
        final_dx = final[:, channels:]
        summed = reduce_everywhere(grad_part, sizes)
        norm_scale = 1.0 / math.sqrt(peer_count * rep_count * owners.shape[0])
        weight_grad = (summed * norm_scale).reshape(27, channels, channels)
        return (final_x[None], final_dx[None], weight_grad)

    return local


def split_space(mesh):
    grid = np.asarray(mesh.devices)
    space_count = grid.shape[0]
    try:
        column = grid[:, 0]
        xs = len({int(d.coords[0]) for d in column})
        cores = len({int(d.core_on_chip) for d in column})
    except Exception:
        cores = 2
        xs = 4
    ys = space_count // (xs * cores)
    return xs, ys, cores


def solution(mesh):
    xs, ys, cores = split_space(mesh)
    grid = np.asarray(mesh.devices)
    rep_count = grid.shape[1]
    fine = Mesh(grid.reshape(xs, ys, cores, rep_count), ("sx", "sy", "sc", "rep"))
    sizes = {"sx": xs, "sy": ys, "sc": cores, "rep": rep_count}
    space = SPACE_AXES
    in_specs = (
        P("rep", space, None),
        P("rep", space, None),
        P("rep", space),
        P("rep", space),
        P("rep", space, None),
        P(),
    )
    out_specs = (P("rep", space, None), P("rep", space, None), P())
    return jax.shard_map(
        make_local(sizes), mesh=fine, in_specs=in_specs, out_specs=out_specs, check_vma=False
    )
```

```python
import math

import jax
import jax.numpy as jnp
import numpy as np
from jax import lax
from jax.sharding import Mesh
from jax.sharding import PartitionSpec as P

NEIGHBOR_OFFSETS = [
    (shift_x, shift_y, shift_z)
    for shift_x in (-1, 0, 1)
    for shift_y in (-1, 0, 1)
    for shift_z in (-1, 0, 1)
    if (shift_x, shift_y, shift_z) != (0, 0, 0)
]
ALL_TAPS = [
    (shift_x, shift_y, shift_z)
    for shift_x in (-1, 0, 1)
    for shift_y in (-1, 0, 1)
    for shift_z in (-1, 0, 1)
]
SPACE_AXES = ("sx", "sy", "sc")
REDUCE_ORDER = ("sc", "sx", "sy", "rep")


def extent(offset):
    if offset < 0:
        return (7, 8)
    if offset == 0:
        return (0, 8)
    return (0, 1)


def pad_blocks(blocks, low_faces, high_faces, slab_links):
    zero_block = jnp.zeros((1,) + blocks.shape[1:], blocks.dtype)
    zero_face = jnp.zeros((1,) + low_faces.shape[1:], low_faces.dtype)
    own_table = jnp.concatenate([blocks, zero_block], 0)
    low_table = jnp.concatenate([low_faces, zero_face], 0)
    high_table = jnp.concatenate([high_faces, zero_face], 0)
    slab_parts = []
    for shift_x in (-1, 0, 1):
        layers = []
        for shift_y in (-1, 0, 1):
            lower_y, upper_y = extent(shift_y)
            pieces = []
            for shift_z in (-1, 0, 1):
                lower_z, upper_z = extent(shift_z)
                if shift_x == 0 and shift_y == 0 and (shift_z == 0):
                    portion = blocks
                else:
                    column = slab_links[:, NEIGHBOR_OFFSETS.index((shift_x, shift_y, shift_z))]
                    if shift_x == 0:
                        portion = own_table[:, :, lower_y:upper_y, lower_z:upper_z][column]
                    elif shift_x < 0:
                        portion = low_table[:, lower_y:upper_y, lower_z:upper_z][column][:, None]
                    else:
                        portion = high_table[:, lower_y:upper_y, lower_z:upper_z][column][:, None]
                pieces.append(portion)
            layers.append(jnp.concatenate(pieces, 3))
        slab_parts.append(jnp.concatenate(layers, 2))
    return jnp.concatenate(slab_parts, 1)


def patch_columns(padded, direction):
    block_count = padded.shape[0]
    channels = padded.shape[-1]
    pieces = []
    for shift_x, shift_y, shift_z in ALL_TAPS:
        start_x = 1 + direction * shift_x
        start_y = 1 + direction * shift_y
        start_z = 1 + direction * shift_z
        pieces.append(
            padded[:, start_x : start_x + 8, start_y : start_y + 8, start_z : start_z + 8, :]
        )
    return jnp.concatenate(pieces, -1).reshape(block_count * 512, 27 * channels)


def tap_view(padded, shift_x, shift_y, shift_z, direction):
    channels = padded.shape[-1]
    start_x = 1 + direction * shift_x
    start_y = 1 + direction * shift_y
    start_z = 1 + direction * shift_z
    return padded[
        :, start_x : start_x + 8, start_y : start_y + 8, start_z : start_z + 8, :
    ].reshape(-1, channels)


def reduce_everywhere(value, sizes, held=None):
    flat = value.reshape(-1)
    for stage, axis in enumerate(REDUCE_ORDER):
        if stage == 1 and held is not None:
            flat, held = lax.optimization_barrier((flat, held))
        count = sizes[axis]
        lanes = 128 if flat.shape[0] % (count * 128) == 0 else flat.shape[0] // count
        parts = lax.all_to_all(flat.reshape(count, -1, lanes), axis, 0, 0, tiled=True)
        flat = jnp.sum(parts, 0).reshape(-1)
    for axis in reversed(REDUCE_ORDER):
        count = sizes[axis]
        lanes = 128 if flat.shape[0] % 128 == 0 else flat.shape[0]
        spread = jnp.broadcast_to(flat.reshape(1, -1, lanes), (count, flat.shape[0] // lanes, lanes))
        flat = lax.all_to_all(spread, axis, 0, 0, tiled=True).reshape(-1)
    return flat.reshape(value.shape), held


def make_local(sizes):
    def local(features, cotangent, point_owner, point_slot, block_links, weights):
        peer_count = sizes["sx"] * sizes["sy"] * sizes["sc"]
        rep_count = sizes["rep"]
        channels = features.shape[-1]
        data_type = features.dtype
        links_here = block_links[0]
        blocks_here = links_here.shape[0]
        voxels = blocks_here * 512
        capacity = voxels // peer_count
        owners = point_owner[0]
        slots_here = point_slot[0]
        matches = (owners[:, None] == jnp.arange(peer_count, dtype=jnp.int32)[None, :]).astype(
            jnp.int32
        )
        earlier = jnp.cumsum(matches, axis=0) - matches
        within = jnp.sum(earlier * matches, axis=1)
        bucket = owners * capacity + within
        payload = jnp.concatenate([features[0], cotangent[0]], -1)
        rows = (
            jnp.zeros((peer_count * capacity, 2 * channels), data_type)
            .at[bucket]
            .set(payload)
            .reshape(peer_count, capacity * 2 * channels)
        )
        slot_full = (
            jnp.full((peer_count * capacity,), voxels, jnp.int32)
            .at[bucket]
            .set(slots_here)
            .reshape(peer_count, capacity)
        )
        slot_hi = (slot_full // 32).astype(data_type)
        slot_lo = (slot_full % 32).astype(data_type)
        slot_row = jnp.concatenate(
            [
                slot_hi,
                slot_lo,
                jnp.zeros((peer_count, 2 * channels - 2 * capacity), data_type),
            ],
            -1,
        )
        send = jnp.concatenate([rows, slot_row], -1)
        recv = lax.all_to_all(send, SPACE_AXES, 0, 0, tiled=True)
        recv_rows = recv[:, : capacity * 2 * channels].reshape(peer_count * capacity, 2 * channels)
        recv_slot = recv[:, capacity * 2 * channels :]
        arrived = (
            recv_slot[:, :capacity].astype(jnp.int32) * 32
            + recv_slot[:, capacity : 2 * capacity].astype(jnp.int32)
        ).reshape(-1)
        dense = (
            jnp.zeros((voxels + 1, 2 * channels), data_type).at[arrived].set(recv_rows)[:voxels]
        )
        dense_x = dense[:, :channels]
        dense_g = dense[:, channels:]
        block_shape = (blocks_here, 8, 8, 8, channels)
        blocks_x = dense_x.reshape(block_shape)
        blocks_h = jnp.maximum(blocks_x, 0)
        blocks_g = dense_g.reshape(block_shape)
        faces = jnp.concatenate(
            [blocks_h[:, 0], blocks_g[:, 0], blocks_h[:, 7], blocks_g[:, 7]], -1
        )
        up = [(i, (i + 1) % peer_count) for i in range(peer_count - 1)]
        down = [(j, i) for i, j in up]
        from_below = lax.ppermute(faces[..., 2 * channels :], SPACE_AXES, up)
        from_above = lax.ppermute(faces[..., : 2 * channels], SPACE_AXES, down)
        low_h, low_g = from_below[..., :channels], from_below[..., channels:]
        high_h, high_g = from_above[..., :channels], from_above[..., channels:]
        padded_h = pad_blocks(blocks_h, low_h, high_h, links_here)
        padded_g = pad_blocks(blocks_g, low_g, high_g, links_here)
        grads_flat = dense_g
        tap_grads = []
        for shift_x, shift_y, shift_z in ALL_TAPS:
            view_h = tap_view(padded_h, shift_x, shift_y, shift_z, 1)
            tap_grads.append(
                lax.dot_general(
                    view_h, grads_flat, (((0,), (0,)), ((), ())), preferred_element_type=jnp.float32
                )
            )
        grad_part = jnp.stack(tap_grads, 0)
        summed, (padded_h, padded_g, dense_x, dense_g) = reduce_everywhere(
            grad_part, sizes, (padded_h, padded_g, dense_x, dense_g)
        )
        convolved = jnp.zeros((voxels, channels), jnp.float32)
        backward = jnp.zeros((voxels, channels), jnp.float32)
        for tap_index, (shift_x, shift_y, shift_z) in enumerate(ALL_TAPS):
            view_h = tap_view(padded_h, shift_x, shift_y, shift_z, 1)
            view_g = tap_view(padded_g, shift_x, shift_y, shift_z, -1)
            tap_weight = weights[tap_index]
            convolved = convolved + jnp.dot(view_h, tap_weight, preferred_element_type=jnp.float32)
            backward = backward + lax.dot_general(
                view_g, tap_weight, (((1,), (1,)), ((), ())), preferred_element_type=jnp.float32
            )
        out_x = (dense_x.astype(jnp.float32) + convolved).astype(data_type)
        out_dx = (dense_g.astype(jnp.float32) + jnp.where(dense_x > 0, backward, 0.0)).astype(
            data_type
        )
        out_both = jnp.concatenate(
            [jnp.concatenate([out_x, out_dx], -1), jnp.zeros((1, 2 * channels), data_type)], 0
        )
        ret = out_both[arrived].reshape(peer_count, capacity * 2 * channels)
        home = lax.all_to_all(ret, SPACE_AXES, 0, 0, tiled=True).reshape(-1, 2 * channels)
        final = home[bucket]
        final_x = final[:, :channels]
        final_dx = final[:, channels:]
        norm_scale = 1.0 / math.sqrt(peer_count * rep_count * owners.shape[0])
        weight_grad = (summed * norm_scale).reshape(27, channels, channels)
        return (final_x[None], final_dx[None], weight_grad)

    return local


def split_space(mesh):
    grid = np.asarray(mesh.devices)
    space_count = grid.shape[0]
    try:
        column = grid[:, 0]
        xs = len({int(d.coords[0]) for d in column})
        cores = len({int(d.core_on_chip) for d in column})
    except Exception:
        cores = 2
        xs = 4
    ys = space_count // (xs * cores)
    return xs, ys, cores


def solution(mesh):
    xs, ys, cores = split_space(mesh)
    grid = np.asarray(mesh.devices)
    rep_count = grid.shape[1]
    fine = Mesh(grid.reshape(xs, ys, cores, rep_count), ("sx", "sy", "sc", "rep"))
    sizes = {"sx": xs, "sy": ys, "sc": cores, "rep": rep_count}
    space = SPACE_AXES
    in_specs = (
        P("rep", space, None),
        P("rep", space, None),
        P("rep", space),
        P("rep", space),
        P("rep", space, None),
        P(),
    )
    out_specs = (P("rep", space, None), P("rep", space, None), P())
    return jax.shard_map(
        make_local(sizes), mesh=fine, in_specs=in_specs, out_specs=out_specs, check_vma=False
    )
```

```python
import math

import jax
import jax.numpy as jnp
import numpy as np
from jax import lax
from jax.sharding import Mesh
from jax.sharding import PartitionSpec as P

NEIGHBOR_OFFSETS = [
    (shift_x, shift_y, shift_z)
    for shift_x in (-1, 0, 1)
    for shift_y in (-1, 0, 1)
    for shift_z in (-1, 0, 1)
    if (shift_x, shift_y, shift_z) != (0, 0, 0)
]
ALL_TAPS = [
    (shift_x, shift_y, shift_z)
    for shift_x in (-1, 0, 1)
    for shift_y in (-1, 0, 1)
    for shift_z in (-1, 0, 1)
]
SPACE_AXES = ("sx", "sy", "sc")
REDUCE_ORDER = ("sc", "sx", "sy", "rep")


def extent(offset):
    if offset < 0:
        return (7, 8)
    if offset == 0:
        return (0, 8)
    return (0, 1)


def pad_blocks(blocks, low_faces, high_faces, slab_links):
    zero_block = jnp.zeros((1,) + blocks.shape[1:], blocks.dtype)
    zero_face = jnp.zeros((1,) + low_faces.shape[1:], low_faces.dtype)
    own_table = jnp.concatenate([blocks, zero_block], 0)
    low_table = jnp.concatenate([low_faces, zero_face], 0)
    high_table = jnp.concatenate([high_faces, zero_face], 0)
    slab_parts = []
    for shift_x in (-1, 0, 1):
        layers = []
        for shift_y in (-1, 0, 1):
            lower_y, upper_y = extent(shift_y)
            pieces = []
            for shift_z in (-1, 0, 1):
                lower_z, upper_z = extent(shift_z)
                if shift_x == 0 and shift_y == 0 and (shift_z == 0):
                    portion = blocks
                else:
                    column = slab_links[:, NEIGHBOR_OFFSETS.index((shift_x, shift_y, shift_z))]
                    if shift_x == 0:
                        portion = own_table[:, :, lower_y:upper_y, lower_z:upper_z][column]
                    elif shift_x < 0:
                        portion = low_table[:, lower_y:upper_y, lower_z:upper_z][column][:, None]
                    else:
                        portion = high_table[:, lower_y:upper_y, lower_z:upper_z][column][:, None]
                pieces.append(portion)
            layers.append(jnp.concatenate(pieces, 3))
        slab_parts.append(jnp.concatenate(layers, 2))
    return jnp.concatenate(slab_parts, 1)


def patch_columns(padded, direction):
    block_count = padded.shape[0]
    channels = padded.shape[-1]
    pieces = []
    for shift_x, shift_y, shift_z in ALL_TAPS:
        start_x = 1 + direction * shift_x
        start_y = 1 + direction * shift_y
        start_z = 1 + direction * shift_z
        pieces.append(
            padded[:, start_x : start_x + 8, start_y : start_y + 8, start_z : start_z + 8, :]
        )
    return jnp.concatenate(pieces, -1).reshape(block_count * 512, 27 * channels)


def tap_view(padded, shift_x, shift_y, shift_z, direction):
    channels = padded.shape[-1]
    start_x = 1 + direction * shift_x
    start_y = 1 + direction * shift_y
    start_z = 1 + direction * shift_z
    return padded[
        :, start_x : start_x + 8, start_y : start_y + 8, start_z : start_z + 8, :
    ].reshape(-1, channels)


def reduce_everywhere(value, sizes, held=None):
    flat = value.reshape(-1)
    lengths = []
    for stage, axis in enumerate(REDUCE_ORDER):
        if stage == 1 and held is not None:
            flat, held = lax.optimization_barrier((flat, held))
        count = sizes[axis]
        lengths.append(flat.shape[0])
        tile = count * 8 * 128
        if flat.shape[0] % tile:
            flat = jnp.pad(flat, (0, tile * (-(-flat.shape[0] // tile)) - flat.shape[0]))
        parts = lax.all_to_all(flat.reshape(count, -1, 128), axis, 0, 0, tiled=True)
        flat = jnp.sum(parts, 0).reshape(-1)
    for axis, length in zip(reversed(REDUCE_ORDER), reversed(lengths)):
        count = sizes[axis]
        spread = jnp.broadcast_to(flat.reshape(1, -1, 128), (count, flat.shape[0] // 128, 128))
        flat = lax.all_to_all(spread, axis, 0, 0, tiled=True).reshape(-1)[:length]
    return flat.reshape(value.shape), held


def make_local(sizes):
    def local(features, cotangent, point_owner, point_slot, block_links, weights):
        peer_count = sizes["sx"] * sizes["sy"] * sizes["sc"]
        rep_count = sizes["rep"]
        channels = features.shape[-1]
        data_type = features.dtype
        links_here = block_links[0]
        blocks_here = links_here.shape[0]
        voxels = blocks_here * 512
        capacity = voxels // peer_count
        owners = point_owner[0]
        slots_here = point_slot[0]
        matches = (owners[:, None] == jnp.arange(peer_count, dtype=jnp.int32)[None, :]).astype(
            jnp.int32
        )
        earlier = jnp.cumsum(matches, axis=0) - matches
        within = jnp.sum(earlier * matches, axis=1)
        bucket = owners * capacity + within
        payload = jnp.concatenate([features[0], cotangent[0]], -1)
        rows = (
            jnp.zeros((peer_count * capacity, 2 * channels), data_type)
            .at[bucket]
            .set(payload)
            .reshape(peer_count, capacity * 2 * channels)
        )
        slot_full = (
            jnp.full((peer_count * capacity,), voxels, jnp.int32)
            .at[bucket]
            .set(slots_here)
            .reshape(peer_count, capacity)
        )
        slot_hi = (slot_full // 32).astype(data_type)
        slot_lo = (slot_full % 32).astype(data_type)
        slot_row = jnp.concatenate(
            [
                slot_hi,
                slot_lo,
                jnp.zeros((peer_count, 2 * channels - 2 * capacity), data_type),
            ],
            -1,
        )
        send = jnp.concatenate([rows, slot_row], -1)
        recv = lax.all_to_all(send, SPACE_AXES, 0, 0, tiled=True)
        recv_rows = recv[:, : capacity * 2 * channels].reshape(peer_count * capacity, 2 * channels)
        recv_slot = recv[:, capacity * 2 * channels :]
        arrived = (
            recv_slot[:, :capacity].astype(jnp.int32) * 32
            + recv_slot[:, capacity : 2 * capacity].astype(jnp.int32)
        ).reshape(-1)
        dense = (
            jnp.zeros((voxels + 1, 2 * channels), data_type).at[arrived].set(recv_rows)[:voxels]
        )
        dense_x = dense[:, :channels]
        dense_g = dense[:, channels:]
        block_shape = (blocks_here, 8, 8, 8, channels)
        blocks_x = dense_x.reshape(block_shape)
        blocks_h = jnp.maximum(blocks_x, 0)
        blocks_g = dense_g.reshape(block_shape)
        faces = jnp.concatenate(
            [blocks_h[:, 0], blocks_g[:, 0], blocks_h[:, 7], blocks_g[:, 7]], -1
        )
        up = [(i, (i + 1) % peer_count) for i in range(peer_count - 1)]
        down = [(j, i) for i, j in up]
        from_below = lax.ppermute(faces[..., 2 * channels :], SPACE_AXES, up)
        from_above = lax.ppermute(faces[..., : 2 * channels], SPACE_AXES, down)
        low_h, low_g = from_below[..., :channels], from_below[..., channels:]
        high_h, high_g = from_above[..., :channels], from_above[..., channels:]
        padded_h = pad_blocks(blocks_h, low_h, high_h, links_here)
        padded_g = pad_blocks(blocks_g, low_g, high_g, links_here)
        grads_flat = dense_g
        tap_grads = []
        for shift_x, shift_y, shift_z in ALL_TAPS:
            view_h = tap_view(padded_h, shift_x, shift_y, shift_z, 1)
            tap_grads.append(
                lax.dot_general(
                    view_h, grads_flat, (((0,), (0,)), ((), ())), preferred_element_type=jnp.float32
                )
            )
        grad_part = jnp.stack(tap_grads, 0)
        summed, (padded_h, padded_g, dense_x, dense_g) = reduce_everywhere(
            grad_part, sizes, (padded_h, padded_g, dense_x, dense_g)
        )
        convolved = jnp.zeros((voxels, channels), jnp.float32)
        backward = jnp.zeros((voxels, channels), jnp.float32)
        for tap_index, (shift_x, shift_y, shift_z) in enumerate(ALL_TAPS):
            view_h = tap_view(padded_h, shift_x, shift_y, shift_z, 1)
            view_g = tap_view(padded_g, shift_x, shift_y, shift_z, -1)
            tap_weight = weights[tap_index]
            convolved = convolved + jnp.dot(view_h, tap_weight, preferred_element_type=jnp.float32)
            backward = backward + lax.dot_general(
                view_g, tap_weight, (((1,), (1,)), ((), ())), preferred_element_type=jnp.float32
            )
        out_x = (dense_x.astype(jnp.float32) + convolved).astype(data_type)
        out_dx = (dense_g.astype(jnp.float32) + jnp.where(dense_x > 0, backward, 0.0)).astype(
            data_type
        )
        out_both = jnp.concatenate(
            [jnp.concatenate([out_x, out_dx], -1), jnp.zeros((1, 2 * channels), data_type)], 0
        )
        ret = out_both[arrived].reshape(peer_count, capacity * 2 * channels)
        home = lax.all_to_all(ret, SPACE_AXES, 0, 0, tiled=True).reshape(-1, 2 * channels)
        final = home[bucket]
        final_x = final[:, :channels]
        final_dx = final[:, channels:]
        norm_scale = 1.0 / math.sqrt(peer_count * rep_count * owners.shape[0])
        weight_grad = (summed * norm_scale).reshape(27, channels, channels)
        return (final_x[None], final_dx[None], weight_grad)

    return local


def split_space(mesh):
    grid = np.asarray(mesh.devices)
    space_count = grid.shape[0]
    try:
        column = grid[:, 0]
        xs = len({int(d.coords[0]) for d in column})
        cores = len({int(d.core_on_chip) for d in column})
    except Exception:
        cores = 2
        xs = 4
    ys = space_count // (xs * cores)
    return xs, ys, cores


def solution(mesh):
    xs, ys, cores = split_space(mesh)
    grid = np.asarray(mesh.devices)
    rep_count = grid.shape[1]
    fine = Mesh(grid.reshape(xs, ys, cores, rep_count), ("sx", "sy", "sc", "rep"))
    sizes = {"sx": xs, "sy": ys, "sc": cores, "rep": rep_count}
    space = SPACE_AXES
    in_specs = (
        P("rep", space, None),
        P("rep", space, None),
        P("rep", space),
        P("rep", space),
        P("rep", space, None),
        P(),
    )
    out_specs = (P("rep", space, None), P("rep", space, None), P())
    return jax.shard_map(
        make_local(sizes), mesh=fine, in_specs=in_specs, out_specs=out_specs, check_vma=False
    )
```

```python
import math

import jax
import jax.numpy as jnp
import numpy as np
from jax import lax
from jax.sharding import Mesh
from jax.sharding import PartitionSpec as P

NEIGHBOR_OFFSETS = [
    (shift_x, shift_y, shift_z)
    for shift_x in (-1, 0, 1)
    for shift_y in (-1, 0, 1)
    for shift_z in (-1, 0, 1)
    if (shift_x, shift_y, shift_z) != (0, 0, 0)
]
ALL_TAPS = [
    (shift_x, shift_y, shift_z)
    for shift_x in (-1, 0, 1)
    for shift_y in (-1, 0, 1)
    for shift_z in (-1, 0, 1)
]
SPACE_AXES = ("sx", "sy", "sc")
REDUCE_ORDER = ("sc", "sx", "sy", "rep")


def extent(offset):
    if offset < 0:
        return (7, 8)
    if offset == 0:
        return (0, 8)
    return (0, 1)


def pad_blocks(blocks, low_faces, high_faces, slab_links):
    zero_block = jnp.zeros((1,) + blocks.shape[1:], blocks.dtype)
    zero_face = jnp.zeros((1,) + low_faces.shape[1:], low_faces.dtype)
    own_table = jnp.concatenate([blocks, zero_block], 0)
    low_table = jnp.concatenate([low_faces, zero_face], 0)
    high_table = jnp.concatenate([high_faces, zero_face], 0)
    slab_parts = []
    for shift_x in (-1, 0, 1):
        layers = []
        for shift_y in (-1, 0, 1):
            lower_y, upper_y = extent(shift_y)
            pieces = []
            for shift_z in (-1, 0, 1):
                lower_z, upper_z = extent(shift_z)
                if shift_x == 0 and shift_y == 0 and (shift_z == 0):
                    portion = blocks
                else:
                    column = slab_links[:, NEIGHBOR_OFFSETS.index((shift_x, shift_y, shift_z))]
                    if shift_x == 0:
                        portion = own_table[:, :, lower_y:upper_y, lower_z:upper_z][column]
                    elif shift_x < 0:
                        portion = low_table[:, lower_y:upper_y, lower_z:upper_z][column][:, None]
                    else:
                        portion = high_table[:, lower_y:upper_y, lower_z:upper_z][column][:, None]
                pieces.append(portion)
            layers.append(jnp.concatenate(pieces, 3))
        slab_parts.append(jnp.concatenate(layers, 2))
    return jnp.concatenate(slab_parts, 1)


def patch_columns(padded, direction):
    block_count = padded.shape[0]
    channels = padded.shape[-1]
    pieces = []
    for shift_x, shift_y, shift_z in ALL_TAPS:
        start_x = 1 + direction * shift_x
        start_y = 1 + direction * shift_y
        start_z = 1 + direction * shift_z
        pieces.append(
            padded[:, start_x : start_x + 8, start_y : start_y + 8, start_z : start_z + 8, :]
        )
    return jnp.concatenate(pieces, -1).reshape(block_count * 512, 27 * channels)


def tap_view(padded, shift_x, shift_y, shift_z, direction):
    channels = padded.shape[-1]
    start_x = 1 + direction * shift_x
    start_y = 1 + direction * shift_y
    start_z = 1 + direction * shift_z
    return padded[
        :, start_x : start_x + 8, start_y : start_y + 8, start_z : start_z + 8, :
    ].reshape(-1, channels)


def reduce_everywhere(value, sizes, held, make_carry):
    flat = value.reshape(-1)
    for stage, axis in enumerate(REDUCE_ORDER):
        if stage == 1:
            flat, held = lax.optimization_barrier((flat, held))
        count = sizes[axis]
        lanes = 128 if flat.shape[0] % (count * 128) == 0 else flat.shape[0] // count
        parts = lax.all_to_all(flat.reshape(count, -1, lanes), axis, 0, 0, tiled=True)
        flat = jnp.sum(parts, 0).reshape(-1)
    carry, carry_axes = None, []
    for axis in reversed(REDUCE_ORDER):
        count = sizes[axis]
        if axis == "sy":
            carry = make_carry(held)
            carry_axes = ["sx", "sy", "sc"]
        lanes = 128 if flat.shape[0] % 128 == 0 else flat.shape[0]
        spread = jnp.broadcast_to(flat.reshape(1, -1, lanes), (count, flat.shape[0] // lanes, lanes))
        if carry is None:
            flat = lax.all_to_all(spread, axis, 0, 0, tiled=True).reshape(-1)
            continue
        where = carry_axes.index(axis)
        order = [where] + [i for i in range(len(carry_axes)) if i != where] + [3]
        carry = jnp.transpose(carry, order)
        carry_axes = [carry_axes[i] for i in order[:3]]
        moved_shape = carry.shape
        rows_here = spread.shape[1]
        sent = jnp.concatenate([spread, carry.reshape(count, -1, 128)], 1)
        got = lax.all_to_all(sent, axis, 0, 0, tiled=True)
        flat = got[:, :rows_here].reshape(-1)
        carry = got[:, rows_here:].reshape(moved_shape)
    order = [carry_axes.index(name) for name in ("sx", "sy", "sc")] + [3]
    home = jnp.transpose(carry, order)
    return flat.reshape(value.shape), held, home


def make_local(sizes):
    def local(features, cotangent, point_owner, point_slot, block_links, weights):
        peer_count = sizes["sx"] * sizes["sy"] * sizes["sc"]
        rep_count = sizes["rep"]
        channels = features.shape[-1]
        data_type = features.dtype
        links_here = block_links[0]
        blocks_here = links_here.shape[0]
        voxels = blocks_here * 512
        capacity = voxels // peer_count
        owners = point_owner[0]
        slots_here = point_slot[0]
        matches = (owners[:, None] == jnp.arange(peer_count, dtype=jnp.int32)[None, :]).astype(
            jnp.int32
        )
        earlier = jnp.cumsum(matches, axis=0) - matches
        within = jnp.sum(earlier * matches, axis=1)
        bucket = owners * capacity + within
        payload = jnp.concatenate([features[0], cotangent[0]], -1)
        rows = (
            jnp.zeros((peer_count * capacity, 2 * channels), data_type)
            .at[bucket]
            .set(payload)
            .reshape(peer_count, capacity * 2 * channels)
        )
        slot_full = (
            jnp.full((peer_count * capacity,), voxels, jnp.int32)
            .at[bucket]
            .set(slots_here)
            .reshape(peer_count, capacity)
        )
        slot_hi = (slot_full // 32).astype(data_type)
        slot_lo = (slot_full % 32).astype(data_type)
        slot_row = jnp.concatenate(
            [
                slot_hi,
                slot_lo,
                jnp.zeros((peer_count, 2 * channels - 2 * capacity), data_type),
            ],
            -1,
        )
        send = jnp.concatenate([rows, slot_row], -1)
        recv = lax.all_to_all(send, SPACE_AXES, 0, 0, tiled=True)
        recv_rows = recv[:, : capacity * 2 * channels].reshape(peer_count * capacity, 2 * channels)
        recv_slot = recv[:, capacity * 2 * channels :]
        arrived = (
            recv_slot[:, :capacity].astype(jnp.int32) * 32
            + recv_slot[:, capacity : 2 * capacity].astype(jnp.int32)
        ).reshape(-1)
        dense = (
            jnp.zeros((voxels + 1, 2 * channels), data_type).at[arrived].set(recv_rows)[:voxels]
        )
        dense_x = dense[:, :channels]
        dense_g = dense[:, channels:]
        block_shape = (blocks_here, 8, 8, 8, channels)
        blocks_x = dense_x.reshape(block_shape)
        blocks_h = jnp.maximum(blocks_x, 0)
        blocks_g = dense_g.reshape(block_shape)
        faces = jnp.concatenate(
            [blocks_h[:, 0], blocks_g[:, 0], blocks_h[:, 7], blocks_g[:, 7]], -1
        )
        up = [(i, (i + 1) % peer_count) for i in range(peer_count - 1)]
        down = [(j, i) for i, j in up]
        from_below = lax.ppermute(faces[..., 2 * channels :], SPACE_AXES, up)
        from_above = lax.ppermute(faces[..., : 2 * channels], SPACE_AXES, down)
        low_h, low_g = from_below[..., :channels], from_below[..., channels:]
        high_h, high_g = from_above[..., :channels], from_above[..., channels:]
        padded_h = pad_blocks(blocks_h, low_h, high_h, links_here)
        padded_g = pad_blocks(blocks_g, low_g, high_g, links_here)
        grads_flat = dense_g
        tap_grads = []
        for shift_x, shift_y, shift_z in ALL_TAPS:
            view_h = tap_view(padded_h, shift_x, shift_y, shift_z, 1)
            tap_grads.append(
                lax.dot_general(
                    view_h, grads_flat, (((0,), (0,)), ((), ())), preferred_element_type=jnp.float32
                )
            )
        grad_part = jnp.stack(tap_grads, 0)
        def make_carry(held):
            padded_h, padded_g, dense_x, dense_g = held
            convolved = jnp.zeros((voxels, channels), jnp.float32)
            backward = jnp.zeros((voxels, channels), jnp.float32)
            for tap_index, (shift_x, shift_y, shift_z) in enumerate(ALL_TAPS):
                view_h = tap_view(padded_h, shift_x, shift_y, shift_z, 1)
                view_g = tap_view(padded_g, shift_x, shift_y, shift_z, -1)
                tap_weight = weights[tap_index]
                convolved = convolved + jnp.dot(view_h, tap_weight, preferred_element_type=jnp.float32)
                backward = backward + lax.dot_general(
                    view_g, tap_weight, (((1,), (1,)), ((), ())), preferred_element_type=jnp.float32
                )
            out_x = (dense_x.astype(jnp.float32) + convolved).astype(data_type)
            out_dx = (dense_g.astype(jnp.float32) + jnp.where(dense_x > 0, backward, 0.0)).astype(
                data_type
            )

            out_both = jnp.concatenate(
                [jnp.concatenate([out_x, out_dx], -1), jnp.zeros((1, 2 * channels), data_type)], 0
            )
            ret = out_both[arrived].astype(jnp.float32)
            return ret.reshape(sizes["sx"], sizes["sy"], sizes["sc"], capacity * 2 * channels)

        summed, _, home = reduce_everywhere(
            grad_part, sizes, (padded_h, padded_g, dense_x, dense_g), make_carry
        )
        home = home.reshape(-1, 2 * channels).astype(data_type)
        final = home[bucket]
        final_x = final[:, :channels]
        final_dx = final[:, channels:]
        norm_scale = 1.0 / math.sqrt(peer_count * rep_count * owners.shape[0])
        weight_grad = (summed * norm_scale).reshape(27, channels, channels)
        return (final_x[None], final_dx[None], weight_grad)

    return local


def split_space(mesh):
    grid = np.asarray(mesh.devices)
    space_count = grid.shape[0]
    try:
        column = grid[:, 0]
        xs = len({int(d.coords[0]) for d in column})
        cores = len({int(d.core_on_chip) for d in column})
    except Exception:
        cores = 2
        xs = 4
    ys = space_count // (xs * cores)
    return xs, ys, cores


def solution(mesh):
    xs, ys, cores = split_space(mesh)
    grid = np.asarray(mesh.devices)
    rep_count = grid.shape[1]
    fine = Mesh(grid.reshape(xs, ys, cores, rep_count), ("sx", "sy", "sc", "rep"))
    sizes = {"sx": xs, "sy": ys, "sc": cores, "rep": rep_count}
    space = SPACE_AXES
    in_specs = (
        P("rep", space, None),
        P("rep", space, None),
        P("rep", space),
        P("rep", space),
        P("rep", space, None),
        P(),
    )
    out_specs = (P("rep", space, None), P("rep", space, None), P())
    return jax.shard_map(
        make_local(sizes), mesh=fine, in_specs=in_specs, out_specs=out_specs, check_vma=False
    )
```

```python
import math

import jax
import jax.numpy as jnp
import numpy as np
from jax import lax
from jax.sharding import Mesh
from jax.sharding import PartitionSpec as P

NEIGHBOR_OFFSETS = [
    (shift_x, shift_y, shift_z)
    for shift_x in (-1, 0, 1)
    for shift_y in (-1, 0, 1)
    for shift_z in (-1, 0, 1)
    if (shift_x, shift_y, shift_z) != (0, 0, 0)
]
ALL_TAPS = [
    (shift_x, shift_y, shift_z)
    for shift_x in (-1, 0, 1)
    for shift_y in (-1, 0, 1)
    for shift_z in (-1, 0, 1)
]
SPACE_AXES = ("sx", "sy", "sc")
REDUCE_ORDER = ("sc", "sx", "sy", "rep")


def extent(offset):
    if offset < 0:
        return (7, 8)
    if offset == 0:
        return (0, 8)
    return (0, 1)


def pad_blocks(blocks, low_faces, high_faces, slab_links):
    zero_block = jnp.zeros((1,) + blocks.shape[1:], blocks.dtype)
    zero_face = jnp.zeros((1,) + low_faces.shape[1:], low_faces.dtype)
    own_table = jnp.concatenate([blocks, zero_block], 0)
    low_table = jnp.concatenate([low_faces, zero_face], 0)
    high_table = jnp.concatenate([high_faces, zero_face], 0)
    slab_parts = []
    for shift_x in (-1, 0, 1):
        layers = []
        for shift_y in (-1, 0, 1):
            lower_y, upper_y = extent(shift_y)
            pieces = []
            for shift_z in (-1, 0, 1):
                lower_z, upper_z = extent(shift_z)
                if shift_x == 0 and shift_y == 0 and (shift_z == 0):
                    portion = blocks
                else:
                    column = slab_links[:, NEIGHBOR_OFFSETS.index((shift_x, shift_y, shift_z))]
                    if shift_x == 0:
                        portion = own_table[:, :, lower_y:upper_y, lower_z:upper_z][column]
                    elif shift_x < 0:
                        portion = low_table[:, lower_y:upper_y, lower_z:upper_z][column][:, None]
                    else:
                        portion = high_table[:, lower_y:upper_y, lower_z:upper_z][column][:, None]
                pieces.append(portion)
            layers.append(jnp.concatenate(pieces, 3))
        slab_parts.append(jnp.concatenate(layers, 2))
    return jnp.concatenate(slab_parts, 1)


def patch_columns(padded, direction):
    block_count = padded.shape[0]
    channels = padded.shape[-1]
    pieces = []
    for shift_x, shift_y, shift_z in ALL_TAPS:
        start_x = 1 + direction * shift_x
        start_y = 1 + direction * shift_y
        start_z = 1 + direction * shift_z
        pieces.append(
            padded[:, start_x : start_x + 8, start_y : start_y + 8, start_z : start_z + 8, :]
        )
    return jnp.concatenate(pieces, -1).reshape(block_count * 512, 27 * channels)


def tap_view(padded, shift_x, shift_y, shift_z, direction):
    channels = padded.shape[-1]
    start_x = 1 + direction * shift_x
    start_y = 1 + direction * shift_y
    start_z = 1 + direction * shift_z
    return padded[
        :, start_x : start_x + 8, start_y : start_y + 8, start_z : start_z + 8, :
    ].reshape(-1, channels)


def reduce_everywhere(value, sizes, held, make_carry, scale):
    flat = value.reshape(-1)
    for stage, axis in enumerate(REDUCE_ORDER):
        if stage == 1:
            flat, held = lax.optimization_barrier((flat, held))
        count = sizes[axis]
        lanes = 128 if flat.shape[0] % (count * 128) == 0 else flat.shape[0] // count
        parts = lax.all_to_all(flat.reshape(count, -1, lanes), axis, 0, 0, tiled=True)
        flat = jnp.sum(parts, 0).reshape(-1)
    flat = flat * scale
    carry, carry_axes = None, []
    for axis in reversed(REDUCE_ORDER):
        count = sizes[axis]
        if axis == "sy":
            carry = make_carry(held)
            carry_axes = ["sx", "sy", "sc"]
        lanes = 128 if flat.shape[0] % 128 == 0 else flat.shape[0]
        spread = jnp.broadcast_to(flat.reshape(1, -1, lanes), (count, flat.shape[0] // lanes, lanes))
        if carry is None:
            flat = lax.all_to_all(spread, axis, 0, 0, tiled=True).reshape(-1)
            continue
        where = carry_axes.index(axis)
        order = [where] + [i for i in range(len(carry_axes)) if i != where] + [3]
        carry = jnp.transpose(carry, order)
        carry_axes = [carry_axes[i] for i in order[:3]]
        moved_shape = carry.shape
        rows_here = spread.shape[1]
        sent = jnp.concatenate([spread, carry.reshape(count, -1, 128)], 1)
        got = lax.all_to_all(sent, axis, 0, 0, tiled=True)
        flat = got[:, :rows_here].reshape(-1)
        carry = got[:, rows_here:].reshape(moved_shape)
    order = [carry_axes.index(name) for name in ("sx", "sy", "sc")] + [3]
    home = jnp.transpose(carry, order)
    return flat.reshape(value.shape), held, home


def make_local(sizes):
    def local(features, cotangent, point_owner, point_slot, block_links, weights):
        peer_count = sizes["sx"] * sizes["sy"] * sizes["sc"]
        rep_count = sizes["rep"]
        channels = features.shape[-1]
        data_type = features.dtype
        links_here = block_links[0]
        blocks_here = links_here.shape[0]
        voxels = blocks_here * 512
        capacity = voxels // peer_count
        owners = point_owner[0]
        slots_here = point_slot[0]
        matches = (owners[:, None] == jnp.arange(peer_count, dtype=jnp.int32)[None, :]).astype(
            jnp.int32
        )
        earlier = jnp.cumsum(matches, axis=0) - matches
        within = jnp.sum(earlier * matches, axis=1)
        bucket = owners * capacity + within
        payload = jnp.concatenate([features[0], cotangent[0]], -1)
        rows = (
            jnp.zeros((peer_count * capacity, 2 * channels), data_type)
            .at[bucket]
            .set(payload)
            .reshape(peer_count, capacity * 2 * channels)
        )
        slot_full = (
            jnp.full((peer_count * capacity,), voxels, jnp.int32)
            .at[bucket]
            .set(slots_here)
            .reshape(peer_count, capacity)
        )
        slot_hi = (slot_full // 32).astype(data_type)
        slot_lo = (slot_full % 32).astype(data_type)
        slot_row = jnp.concatenate(
            [
                slot_hi,
                slot_lo,
                jnp.zeros((peer_count, 2 * channels - 2 * capacity), data_type),
            ],
            -1,
        )
        send = jnp.concatenate([rows, slot_row], -1)
        recv = lax.all_to_all(send, SPACE_AXES, 0, 0, tiled=True)
        recv_rows = recv[:, : capacity * 2 * channels].reshape(peer_count * capacity, 2 * channels)
        recv_slot = recv[:, capacity * 2 * channels :]
        arrived = (
            recv_slot[:, :capacity].astype(jnp.int32) * 32
            + recv_slot[:, capacity : 2 * capacity].astype(jnp.int32)
        ).reshape(-1)
        dense = (
            jnp.zeros((voxels + 1, 2 * channels), data_type).at[arrived].set(recv_rows)[:voxels]
        )
        dense_x = dense[:, :channels]
        dense_g = dense[:, channels:]
        block_shape = (blocks_here, 8, 8, 8, channels)
        blocks_x = dense_x.reshape(block_shape)
        blocks_h = jnp.maximum(blocks_x, 0)
        blocks_g = dense_g.reshape(block_shape)
        faces = jnp.concatenate(
            [blocks_h[:, 0], blocks_g[:, 0], blocks_h[:, 7], blocks_g[:, 7]], -1
        )
        up = [(i, (i + 1) % peer_count) for i in range(peer_count - 1)]
        down = [(j, i) for i, j in up]
        from_below = lax.ppermute(faces[..., 2 * channels :], SPACE_AXES, up)
        from_above = lax.ppermute(faces[..., : 2 * channels], SPACE_AXES, down)
        low_h, low_g = from_below[..., :channels], from_below[..., channels:]
        high_h, high_g = from_above[..., :channels], from_above[..., channels:]
        padded_h = pad_blocks(blocks_h, low_h, high_h, links_here)
        padded_g = pad_blocks(blocks_g, low_g, high_g, links_here)
        grads_flat = dense_g
        tap_grads = []
        for shift_x, shift_y, shift_z in ALL_TAPS:
            view_h = tap_view(padded_h, shift_x, shift_y, shift_z, 1)
            tap_grads.append(
                lax.dot_general(
                    view_h, grads_flat, (((0,), (0,)), ((), ())), preferred_element_type=jnp.float32
                )
            )
        grad_part = jnp.stack(tap_grads, 0)
        def make_carry(held):
            padded_h, padded_g, dense_x, dense_g = held
            convolved = jnp.zeros((voxels, channels), jnp.float32)
            backward = jnp.zeros((voxels, channels), jnp.float32)
            for tap_index, (shift_x, shift_y, shift_z) in enumerate(ALL_TAPS):
                view_h = tap_view(padded_h, shift_x, shift_y, shift_z, 1)
                view_g = tap_view(padded_g, shift_x, shift_y, shift_z, -1)
                tap_weight = weights[tap_index]
                convolved = convolved + jnp.dot(view_h, tap_weight, preferred_element_type=jnp.float32)
                backward = backward + lax.dot_general(
                    view_g, tap_weight, (((1,), (1,)), ((), ())), preferred_element_type=jnp.float32
                )
            out_x = (dense_x.astype(jnp.float32) + convolved).astype(data_type)
            out_dx = (dense_g.astype(jnp.float32) + jnp.where(dense_x > 0, backward, 0.0)).astype(
                data_type
            )

            out_both = jnp.concatenate(
                [jnp.concatenate([out_x, out_dx], -1), jnp.zeros((1, 2 * channels), data_type)], 0
            )
            ret = out_both[arrived].astype(jnp.float32)
            return ret.reshape(sizes["sx"], sizes["sy"], sizes["sc"], capacity * 2 * channels)

        norm_scale = 1.0 / math.sqrt(peer_count * rep_count * owners.shape[0])
        weight_grad, _, home = reduce_everywhere(
            grad_part, sizes, (padded_h, padded_g, dense_x, dense_g), make_carry, norm_scale
        )
        home = home.reshape(-1, 2 * channels).astype(data_type)
        final = home[bucket]
        final_x = final[:, :channels]
        final_dx = final[:, channels:]
        weight_grad = weight_grad.reshape(27, channels, channels)
        return (final_x[None], final_dx[None], weight_grad)

    return local


def split_space(mesh):
    grid = np.asarray(mesh.devices)
    space_count = grid.shape[0]
    try:
        column = grid[:, 0]
        xs = len({int(d.coords[0]) for d in column})
        cores = len({int(d.core_on_chip) for d in column})
    except Exception:
        cores = 2
        xs = 4
    ys = space_count // (xs * cores)
    return xs, ys, cores


def solution(mesh):
    xs, ys, cores = split_space(mesh)
    grid = np.asarray(mesh.devices)
    rep_count = grid.shape[1]
    fine = Mesh(grid.reshape(xs, ys, cores, rep_count), ("sx", "sy", "sc", "rep"))
    sizes = {"sx": xs, "sy": ys, "sc": cores, "rep": rep_count}
    space = SPACE_AXES
    in_specs = (
        P("rep", space, None),
        P("rep", space, None),
        P("rep", space),
        P("rep", space),
        P("rep", space, None),
        P(),
    )
    out_specs = (P("rep", space, None), P("rep", space, None), P())
    return jax.shard_map(
        make_local(sizes), mesh=fine, in_specs=in_specs, out_specs=out_specs, check_vma=False
    )
```
